256 devices in a mesh: dp: 16 (over y, x), section: 2 (over core), tensor: 8 (over z).
Axes of the slice: x: 4, y: 4, z: 8, core: 2. Of those that a mesh axis runs over, the one named last changes fastest.
Arguments:
- tokens: bfloat16 [2048, 16384], P('dp'), may hold values from -9 to 9
- order: int32 [2048], replicated, may hold values from 0 to 2047, as said below
- segments: int32 [2048], replicated, may hold values from 0 to 1, as said below
- gain: float32 [2, 16384], P('section', 'dp'), may hold values from 0.1 to 1.9
- w_query: bfloat16 [2, 16384, 8192], P('section', 'dp', 'tensor'), may hold values from -0.046875 to 0.046875
- key_value_weight: bfloat16 [2, 16384, 8, 256], P('section', 'dp', 'tensor'), may hold values from -0.046875 to 0.046875
- w_out: bfloat16 [2, 8192, 16384], P('section', 'tensor', 'dp'), may hold values from -0.0625 to 0.0625
Outputs:
- layer_out: bfloat16 [2048, 16384], P('section', 'dp')
The draws below stay inside these ranges and needn't reach their ends.
Inputs may be any that keep to these rules, and one draw needn't show every extreme that they name: A permutation that moves whole sentences: the rows of one sentence (a run of equal segments within a block of 32 rows) come from consecutive entry rows in order. `segments`: within each block of 32 rows the sentence numbers do not fall and each of 0 to 1 appears.
All inputs are finite; a program needn't handle non-finite values.
Results may differ from the reference program's by a relative error of at most 0.022.
Values may be sent and summed in bfloat16 or wider, within the bound.
No kernel may reach another device: no remote copies, remote signals or barrier semaphores. Data moves between devices by JAX's collectives and lax.ppermute only.
A program may use at most 64 MiB of HBM per device.

```python
import math
import jax
import jax.numpy as jnp
from jax import lax

MODEL_WIDTH = 16384
HEAD_WIDTH = 128
KEYVALUE_HEADS = 8
QUERY_HEADS = 64
MICRO_TOKENS = 32
M = 4
SENT = 2
TOKENS = 2048
N_DP = 16
N_SECTION = 2
N_TENSOR = 8


def draw_tokens(key, part):
    column = jnp.arange(MODEL_WIDTH, dtype=jnp.float32) / (MODEL_WIDTH - 1)
    scales = 0.35 * jnp.exp(jnp.log(6.0) * column)
    values = jax.random.truncated_normal(jax.random.fold_in(key, 22), -4.0, 4.0, (TOKENS, MODEL_WIDTH), jnp.float32)
    return (values * scales[None, :]).astype(jnp.bfloat16)


def sentence_plan(key):
    block_count = TOKENS // MICRO_TOKENS
    head_lengths = jax.random.randint(jax.random.fold_in(key, 11), (block_count, SENT - 1), 1, MICRO_TOKENS // SENT + 1)
    last_length = MICRO_TOKENS - jnp.sum(head_lengths, axis=1, keepdims=True)
    lengths = jnp.concatenate([head_lengths, last_length], axis=1).astype(jnp.int32)
    bounds = jnp.cumsum(lengths, axis=1)
    position = jnp.arange(MICRO_TOKENS, dtype=jnp.int32)
    sentence_segment_rows = jnp.sum((position[None, :, None] >= bounds[:, None, :SENT - 1]).astype(jnp.int32), axis=2).astype(jnp.int32)
    block_starts = bounds - lengths
    sentence_count = block_count * SENT
    shuffled = jax.random.permutation(jax.random.fold_in(key, 12), sentence_count).astype(jnp.int32)
    flat_lengths = lengths.reshape(-1)
    shuffled_lengths = flat_lengths[shuffled]
    shuffled_starts = (jnp.cumsum(shuffled_lengths) - shuffled_lengths).astype(jnp.int32)
    source_start = jnp.zeros((sentence_count,), jnp.int32).at[shuffled].set(shuffled_starts)
    sentence_ids = jnp.arange(block_count, dtype=jnp.int32)[:, None] * SENT + sentence_segment_rows
    offsets = position[None, :] - jnp.take_along_axis(block_starts, sentence_segment_rows, axis=1)
    order_rows = source_start[sentence_ids] + offsets
    return (order_rows.reshape(-1).astype(jnp.int32), sentence_segment_rows.reshape(-1).astype(jnp.int32))


def draw_order(key, part):
    return sentence_plan(key)[0]


def draw_segments(key, part):
    return sentence_plan(key)[1]


def steps_of(key, dims, cuts, smallest, top_value):
    def one(dim, parts):
        heights = jax.random.uniform(jax.random.fold_in(jax.random.fold_in(key, 6), dim), (parts,), jnp.float32, smallest / len(cuts), top_value / len(cuts))
        return jnp.repeat(jnp.exp(heights), dims[dim] // parts).reshape((-1,) + (1,) * (len(dims) - dim - 1))

    loudness = one(*cuts[0])
    for cut in cuts[1:]:
        loudness = loudness * one(*cut)
    return loudness


def gaussian(rng, shape, deviation, most, shards=(), kind=jnp.bfloat16):
    drawn = jax.random.normal(rng, shape, jnp.float32) * deviation
    if len(shards) > 0:
        drawn = steps_of(rng, shape, shards, -0.22, 0.18) * drawn
    return jnp.clip(drawn, min=-most, max=most).astype(kind)


def setup_inputs(seed: int = 0) -> dict:
    key_of = jax.random.split(jax.random.key(seed), 8)
    tokens = draw_tokens(jax.random.fold_in(key_of[7], 71), 0)
    order = draw_order(jax.random.fold_in(key_of[7], 71), 0)
    segments = draw_segments(jax.random.fold_in(key_of[7], 71), 0)
    gain = jnp.clip(1.0 + 0.18 * jax.random.normal(key_of[3], (N_SECTION, MODEL_WIDTH), jnp.float32), 0.1, 1.9)
    w_query = gaussian(key_of[4], (N_SECTION, MODEL_WIDTH, QUERY_HEADS * HEAD_WIDTH), MODEL_WIDTH ** -0.5, 0.046875, ((0, 2), (1, 16), (2, 8)))
    key_value_weight = gaussian(key_of[5], (N_SECTION, MODEL_WIDTH, KEYVALUE_HEADS, 2 * HEAD_WIDTH), MODEL_WIDTH ** -0.5, 0.046875, ((0, 2), (1, 16), (2, 8)))
    w_out = gaussian(key_of[6], (N_SECTION, QUERY_HEADS * HEAD_WIDTH, MODEL_WIDTH), (QUERY_HEADS * HEAD_WIDTH) ** -0.5, 0.0625, ((0, 2), (1, 8), (2, 16)))
    return {"tokens": tokens, "order": order, "segments": segments, "gain": gain, "w_query": w_query, "key_value_weight": key_value_weight, "w_out": w_out}


norm_epsilon = 1e-05

def attention_blocks(query_rows, key_value_rows, sentence_segment_rows):
    query_group_width = QUERY_HEADS // KEYVALUE_HEADS
    query_head_rows = query_rows.astype(jnp.float32).reshape(N_DP, MICRO_TOKENS, KEYVALUE_HEADS, query_group_width, HEAD_WIDTH)
    query_key_pairs = key_value_rows.astype(jnp.float32).reshape(N_DP, MICRO_TOKENS, KEYVALUE_HEADS, 2 * HEAD_WIDTH)
    key_heads = query_key_pairs[..., :HEAD_WIDTH]
    value_heads = query_key_pairs[..., HEAD_WIDTH:]
    scores = jnp.einsum('bqkgd,bskd->bkgqs', query_head_rows, key_heads) / math.sqrt(HEAD_WIDTH)
    position = jnp.arange(MICRO_TOKENS)
    causal = position[None, :] <= position[:, None]
    allowed = (sentence_segment_rows[:, :, None] == sentence_segment_rows[:, None, :]) & causal[None]
    raw_weights = jnp.where(allowed[:, None, None], jnp.exp(scores), 0.0)
    totals = lax.optimization_barrier(jnp.sum(raw_weights, axis=-1, keepdims=True))
    probs = (raw_weights / totals).astype(jnp.bfloat16)
    attended_rows = jnp.einsum('bkgqs,bskd->bqkgd', probs.astype(jnp.float32), value_heads)
    return attended_rows.astype(jnp.bfloat16).reshape(N_DP * MICRO_TOKENS, QUERY_HEADS * HEAD_WIDTH)

def section_layer(hidden, sentence_segment_rows, gain_row, query_weight, key_value_matrix, out_weight):
    widened = hidden.astype(jnp.float32)
    root_mean_square = jnp.sqrt(lax.optimization_barrier(jnp.sum(widened * widened, axis=1)) / MODEL_WIDTH + norm_epsilon)
    normed_rows = (widened * gain_row[None, :]).astype(jnp.bfloat16)
    query_rows = (jnp.dot(normed_rows, query_weight, preferred_element_type=jnp.float32) / root_mean_square[:, None]).astype(jnp.bfloat16)
    key_value_rows = (jnp.dot(normed_rows, key_value_matrix.reshape(MODEL_WIDTH, KEYVALUE_HEADS * 2 * HEAD_WIDTH), preferred_element_type=jnp.float32) / root_mean_square[:, None]).astype(jnp.bfloat16)
    attended_rows = attention_blocks(query_rows, key_value_rows, sentence_segment_rows)
    block_width = QUERY_HEADS * HEAD_WIDTH // N_TENSOR
    total = jnp.zeros(widened.shape, jnp.float32)
    for tensor_rank in range(N_TENSOR):
        lower = tensor_rank * block_width
        upper = lower + block_width
        partial_term = jnp.dot(attended_rows[:, lower:upper], out_weight[lower:upper], preferred_element_type=jnp.float32)
        rounded = lax.optimization_barrier(partial_term.astype(jnp.bfloat16))
        total = total + rounded.astype(jnp.float32)
    return (widened + total).astype(jnp.bfloat16)

def reference(tokens, order, segments, gain, w_query, key_value_weight, w_out):
    arranged = jnp.take(tokens, order, axis=0)
    rows_all = N_DP * MICRO_TOKENS
    finished = []
    for micro_index in range(M):
        hidden = arranged[micro_index * rows_all:(micro_index + 1) * rows_all]
        sentence_segment_rows = segments[micro_index * rows_all:(micro_index + 1) * rows_all].reshape(N_DP, MICRO_TOKENS)
        for layer_index in range(N_SECTION):
            hidden = section_layer(hidden, sentence_segment_rows, gain[layer_index], w_query[layer_index], key_value_weight[layer_index], w_out[layer_index])
        finished.append(hidden)
    return jnp.concatenate(finished, axis=0)
```

```python
import math

import jax
import jax.numpy as jnp
from jax import lax
from jax.sharding import PartitionSpec as P

MODEL_WIDTH = 16384
KEYVALUE_HEADS = 8
QUERY_HEADS = 64
MICRO_TOKENS = 32
M = 4


norm_epsilon = 1e-05


def causal_block_attend(query_rows, key_value_rows, sentence_segment_rows, query_group_width):
    block_count, row_count = sentence_segment_rows.shape
    kv_heads = key_value_rows.shape[1]
    head_size = key_value_rows.shape[2] // 2
    query_head_rows = query_rows.reshape(
        block_count, row_count, kv_heads, query_group_width, head_size
    )
    key_value_blocks = key_value_rows.reshape(block_count, row_count, kv_heads, 2 * head_size)
    key_heads = key_value_blocks[..., :head_size]
    value_heads = key_value_blocks[..., head_size:]
    scores = jnp.einsum(
        "bqkgd,bskd->bkgqs", query_head_rows, key_heads, preferred_element_type=jnp.float32
    ) / math.sqrt(head_size)
    position = jnp.arange(row_count)
    allowed = (sentence_segment_rows[:, :, None] == sentence_segment_rows[:, None, :]) & (
        position[None, :] <= position[:, None]
    )[None]
    raw_weights = jnp.where(allowed[:, None, None], jnp.exp(scores), 0.0)
    totals = jnp.sum(raw_weights, axis=-1, keepdims=True)
    probs = (raw_weights / totals).astype(jnp.bfloat16)
    attended_rows = jnp.einsum(
        "bkgqs,bskd->bqkgd", probs, value_heads, preferred_element_type=jnp.float32
    )
    return attended_rows.astype(jnp.bfloat16).reshape(
        block_count * row_count, kv_heads * query_group_width * head_size
    )


def section_layer(
    hidden, sentence_segment_rows, gain_row, query_weight, key_value_matrix, out_weight
):
    slice_width = hidden.shape[1]
    row_count = hidden.shape[0]
    widened = hidden.astype(jnp.float32)
    normed_rows = (widened * gain_row[None, :]).astype(jnp.bfloat16)
    query_terms = jnp.dot(normed_rows, query_weight, preferred_element_type=jnp.float32)
    keyval_terms = jnp.dot(
        normed_rows, key_value_matrix.reshape(slice_width, -1), preferred_element_type=jnp.float32
    )
    query_width = query_terms.shape[1]
    square_terms = jnp.sum(widened * widened, axis=1)
    all_squares = lax.psum(square_terms, "dp")
    joined_sums = lax.psum(
        jnp.concatenate([query_terms, keyval_terms], axis=1).astype(jnp.bfloat16), "dp"
    ).astype(jnp.float32)
    root_mean_square = jnp.sqrt(all_squares / MODEL_WIDTH + norm_epsilon)
    scaled_sums = joined_sums / root_mean_square[:, None]
    query_rows = scaled_sums[:, :query_width].astype(jnp.bfloat16)
    kv_heads = key_value_matrix.shape[1]
    key_value_rows = (
        scaled_sums[:, query_width:]
        .astype(jnp.bfloat16)
        .reshape(row_count, kv_heads, key_value_matrix.shape[2])
    )
    attended_rows = causal_block_attend(
        query_rows, key_value_rows, sentence_segment_rows, QUERY_HEADS // KEYVALUE_HEADS
    )
    head_terms = jnp.dot(attended_rows, out_weight, preferred_element_type=jnp.float32)
    head_total = lax.psum(head_terms.astype(jnp.bfloat16), "tensor").astype(jnp.float32)
    return (widened + head_total).astype(jnp.bfloat16)


def on_device(tokens, order, segments, gain, w_query, key_value_weight, w_out):
    section_count = lax.axis_size("section")
    section_index = lax.axis_index("section")
    own = (gain[0], w_query[0], key_value_weight[0], w_out[0])
    other = lax.ppermute(own, "section", [(i, (i + 1) % section_count) for i in range(section_count)])
    spread = lax.all_to_all(tokens, "dp", split_axis=1, concat_axis=0, tiled=True)
    rows_here = spread.shape[0] // section_count
    my_order = lax.dynamic_slice_in_dim(order, section_index * rows_here, rows_here)
    hidden = jnp.take(spread, my_order, axis=0)
    my_segments = lax.dynamic_slice_in_dim(
        segments, section_index * rows_here, rows_here
    ).reshape(-1, MICRO_TOKENS)
    for layer_index in range(section_count):
        params = jax.tree.map(
            lambda mine, theirs: jnp.where(section_index == layer_index, mine, theirs), own, other
        )
        hidden = section_layer(hidden, my_segments, *params)
    return hidden


def solution(mesh):
    placed = (
        P("dp", None),
        P(),
        P(),
        P("section", "dp"),
        P("section", "dp", "tensor"),
        P("section", "dp", "tensor", None),
        P("section", "tensor", "dp"),
    )
    return jax.shard_map(
        on_device, mesh=mesh, in_specs=placed, out_specs=P("section", "dp"), check_vma=False
    )
```

```python
import math

import jax
import jax.numpy as jnp
from jax import lax
from jax.sharding import PartitionSpec as P

MODEL_WIDTH = 16384
KEYVALUE_HEADS = 8
QUERY_HEADS = 64
MICRO_TOKENS = 32
M = 4


norm_epsilon = 1e-05


def causal_block_attend(query_rows, key_value_rows, sentence_segment_rows, query_group_width):
    block_count, row_count = sentence_segment_rows.shape
    kv_heads = key_value_rows.shape[1]
    head_size = key_value_rows.shape[2] // 2
    query_head_rows = query_rows.reshape(
        block_count, row_count, kv_heads, query_group_width, head_size
    )
    key_value_blocks = key_value_rows.reshape(block_count, row_count, kv_heads, 2 * head_size)
    key_heads = key_value_blocks[..., :head_size]
    value_heads = key_value_blocks[..., head_size:]
    scores = jnp.einsum(
        "bqkgd,bskd->bkgqs", query_head_rows, key_heads, preferred_element_type=jnp.float32
    ) / math.sqrt(head_size)
    position = jnp.arange(row_count)
    allowed = (sentence_segment_rows[:, :, None] == sentence_segment_rows[:, None, :]) & (
        position[None, :] <= position[:, None]
    )[None]
    raw_weights = jnp.where(allowed[:, None, None], jnp.exp(scores), 0.0)
    totals = jnp.sum(raw_weights, axis=-1, keepdims=True)
    probs = (raw_weights / totals).astype(jnp.bfloat16)
    attended_rows = jnp.einsum(
        "bkgqs,bskd->bqkgd", probs, value_heads, preferred_element_type=jnp.float32
    )
    return attended_rows.astype(jnp.bfloat16).reshape(
        block_count * row_count, kv_heads * query_group_width * head_size
    )


def gathered_over(block, axis):
    count = lax.axis_size(axis)
    spread = jnp.broadcast_to(block[None], (count,) + block.shape)
    return lax.all_to_all(spread, axis, 0, 0, tiled=False).reshape(
        (count * block.shape[0],) + block.shape[1:]
    )


def section_layer(
    hidden, sentence_segment_rows, gain_row, query_weight, key_value_matrix, out_weight
):
    slice_width = hidden.shape[1]
    row_count = hidden.shape[0]
    group_count = lax.axis_size("dp")
    own_rows = row_count // group_count
    own_blocks = own_rows // MICRO_TOKENS
    own_segments = lax.dynamic_slice_in_dim(
        sentence_segment_rows, lax.axis_index("dp") * own_blocks, own_blocks
    )
    widened = hidden.astype(jnp.float32)
    normed_rows = (widened * gain_row[None, :]).astype(jnp.bfloat16)
    query_terms = jnp.dot(normed_rows, query_weight, preferred_element_type=jnp.float32)
    keyval_terms = jnp.dot(
        normed_rows, key_value_matrix.reshape(slice_width, -1), preferred_element_type=jnp.float32
    )
    query_width = query_terms.shape[1]
    keyval_width = keyval_terms.shape[1]
    square_terms = jnp.sum(widened * widened, axis=1, keepdims=True)
    square_high = lax.reduce_precision(square_terms, exponent_bits=8, mantissa_bits=7)
    square_low = square_terms - square_high
    payload = jnp.concatenate(
        [
            query_terms.astype(jnp.bfloat16),
            keyval_terms.astype(jnp.bfloat16),
            square_high.astype(jnp.bfloat16),
            square_low.astype(jnp.bfloat16),
            jnp.zeros((row_count, 126), jnp.bfloat16),
        ],
        axis=1,
    )
    arrived = lax.all_to_all(
        payload.reshape(group_count, own_rows, payload.shape[1]), "dp", 0, 0, tiled=False
    )
    summed = jnp.sum(arrived.astype(jnp.float32), axis=0)
    own_squares = summed[:, query_width + keyval_width] + summed[:, query_width + keyval_width + 1]
    root_mean_square = jnp.sqrt(own_squares / MODEL_WIDTH + norm_epsilon)
    scaled_sums = summed[:, : query_width + keyval_width] / root_mean_square[:, None]
    query_rows = scaled_sums[:, :query_width].astype(jnp.bfloat16)
    kv_heads = key_value_matrix.shape[1]
    key_value_rows = (
        scaled_sums[:, query_width:]
        .astype(jnp.bfloat16)
        .reshape(own_rows, kv_heads, key_value_matrix.shape[2])
    )
    attended_rows = causal_block_attend(
        query_rows, key_value_rows, own_segments, QUERY_HEADS // KEYVALUE_HEADS
    )
    head_terms = jnp.dot(
        gathered_over(attended_rows, "dp"), out_weight, preferred_element_type=jnp.float32
    )
    head_total = lax.psum(head_terms.astype(jnp.bfloat16), "tensor").astype(jnp.float32)
    return (widened + head_total).astype(jnp.bfloat16)


def on_device(tokens, order, segments, gain, w_query, key_value_weight, w_out):
    section_count = lax.axis_size("section")
    section_index = lax.axis_index("section")
    group_count = lax.axis_size("dp")
    own = (gain[0], w_query[0], key_value_weight[0], w_out[0])
    swap = [(i, (i + 1) % section_count) for i in range(section_count)]
    other = lax.ppermute(own, "section", swap)
    entry_rows, model_width = tokens.shape
    slice_width = model_width // group_count
    half_width = slice_width // section_count
    my_columns = lax.dynamic_slice_in_dim(
        tokens.reshape(entry_rows, group_count, section_count, half_width),
        section_index,
        1,
        axis=2,
    ).reshape(entry_rows, group_count, half_width)
    spread = lax.all_to_all(my_columns, "dp", 1, 0, tiled=True).reshape(-1, half_width)
    arranged = jnp.take(spread, order, axis=0)
    rows_here = arranged.shape[0] // section_count
    both = arranged.reshape(section_count, rows_here, half_width)
    mine = lax.dynamic_index_in_dim(both, section_index, 0, keepdims=False)
    theirs = lax.dynamic_index_in_dim(both, 1 - section_index, 0, keepdims=False)
    received = lax.ppermute(theirs, "section", swap)
    hidden = jnp.where(
        section_index == 0,
        jnp.concatenate([mine, received], axis=1),
        jnp.concatenate([received, mine], axis=1),
    )
    my_segments = lax.dynamic_slice_in_dim(
        segments, section_index * rows_here, rows_here
    ).reshape(-1, MICRO_TOKENS)
    for layer_index in range(section_count):
        params = jax.tree.map(
            lambda mine, theirs: jnp.where(section_index == layer_index, mine, theirs), own, other
        )
        hidden = section_layer(hidden, my_segments, *params)
    return hidden


def solution(mesh):
    placed = (
        P("dp", None),
        P(),
        P(),
        P("section", "dp"),
        P("section", "dp", "tensor"),
        P("section", "dp", "tensor", None),
        P("section", "tensor", "dp"),
    )
    return jax.shard_map(
        on_device, mesh=mesh, in_specs=placed, out_specs=P("section", "dp"), check_vma=False
    )
```

```python
import math

import jax
import jax.numpy as jnp
from jax import lax
from jax.sharding import PartitionSpec as P

MODEL_WIDTH = 16384
KEYVALUE_HEADS = 8
QUERY_HEADS = 64
MICRO_TOKENS = 32
HEAD_WIDTH = 128
M = 4


norm_epsilon = 1e-05


def causal_block_attend(query_rows, key_value_rows, sentence_segment_rows, query_group_width):
    block_count, row_count = sentence_segment_rows.shape
    kv_heads = key_value_rows.shape[1]
    head_size = key_value_rows.shape[2] // 2
    query_head_rows = query_rows.reshape(
        block_count, row_count, kv_heads, query_group_width, head_size
    )
    key_value_blocks = key_value_rows.reshape(block_count, row_count, kv_heads, 2 * head_size)
    key_heads = key_value_blocks[..., :head_size]
    value_heads = key_value_blocks[..., head_size:]
    scores = jnp.einsum(
        "bqkgd,bskd->bkgqs", query_head_rows, key_heads, preferred_element_type=jnp.float32
    ) / math.sqrt(head_size)
    position = jnp.arange(row_count)
    allowed = (sentence_segment_rows[:, :, None] == sentence_segment_rows[:, None, :]) & (
        position[None, :] <= position[:, None]
    )[None]
    raw_weights = jnp.where(allowed[:, None, None], jnp.exp(scores), 0.0)
    totals = jnp.sum(raw_weights, axis=-1, keepdims=True)
    probs = (raw_weights / totals).astype(jnp.bfloat16)
    attended_rows = jnp.einsum(
        "bkgqs,bskd->bqkgd", probs, value_heads, preferred_element_type=jnp.float32
    )
    return attended_rows.astype(jnp.bfloat16).reshape(
        block_count * row_count, kv_heads * query_group_width * head_size
    )


def gathered_over(block, axis):
    count = lax.axis_size(axis)
    spread = jnp.broadcast_to(block[None], (count,) + block.shape)
    return lax.all_to_all(spread, axis, 0, 0, tiled=False).reshape(
        (count * block.shape[0],) + block.shape[1:]
    )


def section_layer(hidden, sentence_segment_rows, gain_row, joined_weight, out_weight):
    slice_width = hidden.shape[1]
    row_count = hidden.shape[0]
    group_count = lax.axis_size("dp")
    own_rows = row_count // group_count
    own_blocks = own_rows // MICRO_TOKENS
    own_segments = lax.dynamic_slice_in_dim(
        sentence_segment_rows, lax.axis_index("dp") * own_blocks, own_blocks
    )
    widened = hidden.astype(jnp.float32)
    normed_rows = (widened * gain_row[None, :]).astype(jnp.bfloat16)
    joined_terms = jnp.dot(normed_rows, joined_weight, preferred_element_type=jnp.float32)
    query_width = out_weight.shape[0]
    keyval_width = joined_terms.shape[1] - query_width
    square_terms = jnp.sum(widened * widened, axis=1, keepdims=True)
    square_high = lax.reduce_precision(square_terms, exponent_bits=8, mantissa_bits=7)
    square_low = square_terms - square_high
    payload = jnp.concatenate(
        [
            joined_terms.astype(jnp.bfloat16),
            square_high.astype(jnp.bfloat16),
            square_low.astype(jnp.bfloat16),
            jnp.zeros((row_count, 126), jnp.bfloat16),
        ],
        axis=1,
    )
    arrived = lax.all_to_all(
        payload.reshape(group_count, own_rows, payload.shape[1]), "dp", 0, 0, tiled=False
    )
    summed = jnp.sum(arrived.astype(jnp.float32), axis=0)
    own_squares = summed[:, query_width + keyval_width] + summed[:, query_width + keyval_width + 1]
    root_mean_square = jnp.sqrt(own_squares / MODEL_WIDTH + norm_epsilon)
    scaled_sums = summed[:, : query_width + keyval_width] / root_mean_square[:, None]
    query_rows = scaled_sums[:, :query_width].astype(jnp.bfloat16)
    key_value_rows = (
        scaled_sums[:, query_width:]
        .astype(jnp.bfloat16)
        .reshape(own_rows, -1, 2 * HEAD_WIDTH)
    )
    attended_rows = causal_block_attend(
        query_rows, key_value_rows, own_segments, QUERY_HEADS // KEYVALUE_HEADS
    )
    head_terms = jnp.dot(
        gathered_over(attended_rows, "dp"), out_weight, preferred_element_type=jnp.float32
    )
    head_total = lax.psum(head_terms.astype(jnp.bfloat16), "tensor").astype(jnp.float32)
    return (widened + head_total).astype(jnp.bfloat16)


def on_device(tokens, order, segments, gain, w_query, key_value_weight, w_out):
    section_count = lax.axis_size("section")
    section_index = lax.axis_index("section")
    group_count = lax.axis_size("dp")
    slice_width = w_query.shape[1]
    joined = jnp.concatenate(
        [w_query[0], key_value_weight[0].reshape(slice_width, -1)], axis=1
    )
    own = (gain[0], joined, w_out[0])
    swap = [(i, (i + 1) % section_count) for i in range(section_count)]
    other = lax.ppermute(own, "section", swap)
    entry_rows, model_width = tokens.shape
    part_rows = entry_rows // section_count
    my_rows = lax.dynamic_slice_in_dim(tokens, section_index * part_rows, part_rows)
    got = lax.all_to_all(
        my_rows.reshape(part_rows, group_count, model_width // group_count), "dp", 1, 0, tiled=True
    ).reshape(group_count * part_rows, -1)
    received = lax.ppermute(got, "section", swap)
    pool = jnp.concatenate([got, received], axis=0)
    rows_here = group_count * entry_rows // section_count
    my_order = lax.dynamic_slice_in_dim(order, section_index * rows_here, rows_here)
    source_group = my_order // entry_rows
    within = my_order % entry_rows
    from_other = (within // part_rows) != section_index
    pool_index = (
        jnp.where(from_other, group_count * part_rows, 0)
        + source_group * part_rows
        + within % part_rows
    )
    hidden = jnp.take(pool, pool_index, axis=0)
    my_segments = lax.dynamic_slice_in_dim(
        segments, section_index * rows_here, rows_here
    ).reshape(-1, MICRO_TOKENS)
    for layer_index in range(section_count):
        params = jax.tree.map(
            lambda mine, theirs: jnp.where(section_index == layer_index, mine, theirs), own, other
        )
        hidden = section_layer(hidden, my_segments, *params)
    return hidden


def solution(mesh):
    placed = (
        P("dp", None),
        P(),
        P(),
        P("section", "dp"),
        P("section", "dp", "tensor"),
        P("section", "dp", "tensor", None),
        P("section", "tensor", "dp"),
    )
    return jax.shard_map(
        on_device, mesh=mesh, in_specs=placed, out_specs=P("section", "dp"), check_vma=False
    )
```

```python
import math

import jax
import jax.numpy as jnp
from jax import lax
from jax.sharding import PartitionSpec as P

MODEL_WIDTH = 16384
KEYVALUE_HEADS = 8
QUERY_HEADS = 64
MICRO_TOKENS = 32
HEAD_WIDTH = 128
SPARE_COLUMNS = 128
M = 4


norm_epsilon = 1e-05


def causal_block_attend(query_rows, key_value_rows, sentence_segment_rows, query_group_width):
    block_count, row_count = sentence_segment_rows.shape
    kv_heads = key_value_rows.shape[1]
    head_size = key_value_rows.shape[2] // 2
    query_head_rows = query_rows.reshape(
        block_count, row_count, kv_heads, query_group_width, head_size
    )
    key_value_blocks = key_value_rows.reshape(block_count, row_count, kv_heads, 2 * head_size)
    key_heads = key_value_blocks[..., :head_size]
    value_heads = key_value_blocks[..., head_size:]
    scores = jnp.einsum(
        "bqkgd,bskd->bkgqs", query_head_rows, key_heads, preferred_element_type=jnp.float32
    ) / math.sqrt(head_size)
    position = jnp.arange(row_count)
    allowed = (sentence_segment_rows[:, :, None] == sentence_segment_rows[:, None, :]) & (
        position[None, :] <= position[:, None]
    )[None]
    raw_weights = jnp.where(allowed[:, None, None], jnp.exp(scores), 0.0)
    totals = jnp.sum(raw_weights, axis=-1, keepdims=True)
    probs = (raw_weights / totals).astype(jnp.bfloat16)
    attended_rows = jnp.einsum(
        "bkgqs,bskd->bqkgd", probs, value_heads, preferred_element_type=jnp.float32
    )
    return attended_rows.astype(jnp.bfloat16).reshape(
        block_count * row_count, kv_heads * query_group_width * head_size
    )


def gathered_over(block, axis):
    count = lax.axis_size(axis)
    spread = jnp.broadcast_to(block[None], (count,) + block.shape)
    return lax.all_to_all(spread, axis, 0, 0, tiled=False).reshape(
        (count * block.shape[0],) + block.shape[1:]
    )


def section_layer(hidden, sentence_segment_rows, gain_row, joined_weight, out_weight):
    slice_width = hidden.shape[1]
    row_count = hidden.shape[0]
    group_count = lax.axis_size("dp")
    own_rows = row_count // group_count
    own_blocks = own_rows // MICRO_TOKENS
    own_segments = lax.dynamic_slice_in_dim(
        sentence_segment_rows, lax.axis_index("dp") * own_blocks, own_blocks
    )
    widened = hidden.astype(jnp.float32)
    normed_rows = (widened * gain_row[None, :]).astype(jnp.bfloat16)
    joined_terms = jnp.dot(normed_rows, joined_weight, preferred_element_type=jnp.float32)
    query_width = out_weight.shape[0]
    keyval_width = joined_terms.shape[1] - query_width - SPARE_COLUMNS
    square_terms = jnp.sum(widened * widened, axis=1, keepdims=True)
    square_high = lax.reduce_precision(square_terms, exponent_bits=8, mantissa_bits=7)
    square_low = square_terms - square_high
    column = lax.broadcasted_iota(jnp.int32, joined_terms.shape, 1)
    square_column = query_width + keyval_width
    payload = jnp.where(
        column == square_column,
        square_high,
        jnp.where(column == square_column + 1, square_low, joined_terms),
    ).astype(jnp.bfloat16)
    arrived = lax.all_to_all(
        payload.reshape(group_count, own_rows, payload.shape[1]), "dp", 0, 0, tiled=False
    )
    summed = jnp.sum(arrived.astype(jnp.float32), axis=0)
    own_squares = summed[:, query_width + keyval_width] + summed[:, query_width + keyval_width + 1]
    root_mean_square = jnp.sqrt(own_squares / MODEL_WIDTH + norm_epsilon)
    scaled_sums = summed[:, : query_width + keyval_width] / root_mean_square[:, None]
    query_rows = scaled_sums[:, :query_width].astype(jnp.bfloat16)
    key_value_rows = (
        scaled_sums[:, query_width:]
        .astype(jnp.bfloat16)
        .reshape(own_rows, -1, 2 * HEAD_WIDTH)
    )
    attended_rows = causal_block_attend(
        query_rows, key_value_rows, own_segments, QUERY_HEADS // KEYVALUE_HEADS
    )
    head_terms = jnp.dot(
        gathered_over(attended_rows, "dp"), out_weight, preferred_element_type=jnp.float32
    )
    head_total = lax.psum(head_terms.astype(jnp.bfloat16), "tensor").astype(jnp.float32)
    return (widened + head_total).astype(jnp.bfloat16)


def on_device(tokens, order, segments, gain, w_query, key_value_weight, w_out):
    section_count = lax.axis_size("section")
    section_index = lax.axis_index("section")
    group_count = lax.axis_size("dp")
    slice_width = w_query.shape[1]
    joined = jnp.concatenate(
        [
            w_query[0],
            key_value_weight[0].reshape(slice_width, -1),
            jnp.zeros((slice_width, SPARE_COLUMNS), w_query.dtype),
        ],
        axis=1,
    )
    own = (gain[0], joined, w_out[0])
    swap = [(i, (i + 1) % section_count) for i in range(section_count)]
    other = lax.ppermute(own, "section", swap)
    entry_rows, model_width = tokens.shape
    part_rows = entry_rows // section_count
    my_rows = lax.dynamic_slice_in_dim(tokens, section_index * part_rows, part_rows)
    got = lax.all_to_all(
        my_rows.reshape(part_rows, group_count, model_width // group_count), "dp", 1, 0, tiled=True
    ).reshape(group_count * part_rows, -1)
    received = lax.ppermute(got, "section", swap)
    pool = jnp.concatenate([got, received], axis=0)
    rows_here = group_count * entry_rows // section_count
    my_order = lax.dynamic_slice_in_dim(order, section_index * rows_here, rows_here)
    source_group = my_order // entry_rows
    within = my_order % entry_rows
    from_other = (within // part_rows) != section_index
    pool_index = (
        jnp.where(from_other, group_count * part_rows, 0)
        + source_group * part_rows
        + within % part_rows
    )
    hidden = jnp.take(pool, pool_index, axis=0)
    my_segments = lax.dynamic_slice_in_dim(
        segments, section_index * rows_here, rows_here
    ).reshape(-1, MICRO_TOKENS)
    for layer_index in range(section_count):
        params = jax.tree.map(
            lambda mine, theirs: jnp.where(section_index == layer_index, mine, theirs), own, other
        )
        hidden = section_layer(hidden, my_segments, *params)
    return hidden


def solution(mesh):
    placed = (
        P("dp", None),
        P(),
        P(),
        P("section", "dp"),
        P("section", "dp", "tensor"),
        P("section", "dp", "tensor", None),
        P("section", "tensor", "dp"),
    )
    return jax.shard_map(
        on_device, mesh=mesh, in_specs=placed, out_specs=P("section", "dp"), check_vma=False
    )
```

```python
import math

import jax
import jax.numpy as jnp
from jax import lax
from jax.sharding import PartitionSpec as P

MODEL_WIDTH = 16384
KEYVALUE_HEADS = 8
QUERY_HEADS = 64
MICRO_TOKENS = 32
HEAD_WIDTH = 128
SPARE_COLUMNS = 128
M = 4


norm_epsilon = 1e-05


def causal_block_attend(query_rows, key_value_rows, allowed, query_group_width):
    block_count, row_count = allowed.shape[:2]
    kv_heads = key_value_rows.shape[1]
    head_size = key_value_rows.shape[2] // 2
    query_head_rows = query_rows.reshape(
        block_count, row_count, kv_heads, query_group_width, head_size
    )
    key_value_blocks = key_value_rows.reshape(block_count, row_count, kv_heads, 2 * head_size)
    key_heads = key_value_blocks[..., :head_size]
    value_heads = key_value_blocks[..., head_size:]
    scores = jnp.einsum(
        "bqkgd,bskd->bkgqs", query_head_rows, key_heads, preferred_element_type=jnp.float32
    ) / math.sqrt(head_size)
    raw_weights = jnp.where(allowed[:, None, None], jnp.exp(scores), 0.0)
    totals = jnp.sum(raw_weights, axis=-1, keepdims=True)
    probs = (raw_weights / totals).astype(jnp.bfloat16)
    attended_rows = jnp.einsum(
        "bkgqs,bskd->bqkgd", probs, value_heads, preferred_element_type=jnp.float32
    )
    return attended_rows.astype(jnp.bfloat16).reshape(
        block_count * row_count, kv_heads * query_group_width * head_size
    )


def block_mask(sentence_segment_rows):
    row_count = sentence_segment_rows.shape[1]
    position = jnp.arange(row_count)
    return (sentence_segment_rows[:, :, None] == sentence_segment_rows[:, None, :]) & (
        position[None, :] <= position[:, None]
    )[None]


def gathered_over(block, axis):
    count = lax.axis_size(axis)
    spread = jnp.broadcast_to(block[None], (count,) + block.shape)
    return lax.all_to_all(spread, axis, 0, 0, tiled=False).reshape(
        (count * block.shape[0],) + block.shape[1:]
    )


def section_layer(hidden, own_allowed, gain_row, joined_weight, out_weight):
    row_count = hidden.shape[0]
    group_count = lax.axis_size("dp")
    own_rows = row_count // group_count
    widened = hidden.astype(jnp.float32)
    normed_rows = (widened * gain_row[None, :]).astype(jnp.bfloat16)
    joined_terms = jnp.dot(normed_rows, joined_weight, preferred_element_type=jnp.float32)
    query_width = out_weight.shape[0]
    keyval_width = joined_terms.shape[1] - query_width - SPARE_COLUMNS
    square_terms = jnp.sum(widened * widened, axis=1, keepdims=True)
    square_high = lax.reduce_precision(square_terms, exponent_bits=8, mantissa_bits=7)
    square_low = square_terms - square_high
    column = lax.broadcasted_iota(jnp.int32, joined_terms.shape, 1)
    square_column = query_width + keyval_width
    payload = jnp.where(
        column == square_column,
        square_high,
        jnp.where(column == square_column + 1, square_low, joined_terms),
    ).astype(jnp.bfloat16)
    arrived = lax.all_to_all(
        payload.reshape(group_count, own_rows, payload.shape[1]), "dp", 0, 0, tiled=False
    )
    summed = jnp.sum(arrived.astype(jnp.float32), axis=0)
    own_squares = summed[:, query_width + keyval_width] + summed[:, query_width + keyval_width + 1]
    root_mean_square = jnp.sqrt(own_squares / MODEL_WIDTH + norm_epsilon)
    scaled_sums = summed[:, : query_width + keyval_width] / root_mean_square[:, None]
    query_rows = scaled_sums[:, :query_width].astype(jnp.bfloat16)
    key_value_rows = (
        scaled_sums[:, query_width:]
        .astype(jnp.bfloat16)
        .reshape(own_rows, -1, 2 * HEAD_WIDTH)
    )
    attended_rows = causal_block_attend(
        query_rows, key_value_rows, own_allowed, QUERY_HEADS // KEYVALUE_HEADS
    )
    head_terms = jnp.dot(
        gathered_over(attended_rows, "dp"), out_weight, preferred_element_type=jnp.float32
    )
    head_total = lax.psum(head_terms.astype(jnp.bfloat16), "tensor").astype(jnp.float32)
    return (widened + head_total).astype(jnp.bfloat16)


def on_device(tokens, order, segments, gain, w_query, key_value_weight, w_out):
    section_count = lax.axis_size("section")
    section_index = lax.axis_index("section")
    group_count = lax.axis_size("dp")
    slice_width = w_query.shape[1]
    joined = jnp.concatenate(
        [
            w_query[0],
            key_value_weight[0].reshape(slice_width, -1),
            jnp.zeros((slice_width, SPARE_COLUMNS), w_query.dtype),
        ],
        axis=1,
    )
    own = (gain[0], joined, w_out[0])
    swap = [(i, (i + 1) % section_count) for i in range(section_count)]
    other = lax.ppermute(own, "section", swap)
    entry_rows, model_width = tokens.shape
    part_rows = entry_rows // section_count
    my_rows = lax.dynamic_slice_in_dim(tokens, section_index * part_rows, part_rows)
    got = lax.all_to_all(
        my_rows.reshape(part_rows, group_count, model_width // group_count), "dp", 1, 0, tiled=True
    ).reshape(group_count * part_rows, -1)
    received = lax.ppermute(got, "section", swap)
    rows_here = group_count * entry_rows // section_count
    own_blocks = rows_here // (group_count * MICRO_TOKENS)
    own_segments = lax.dynamic_slice_in_dim(
        segments,
        section_index * rows_here + lax.axis_index("dp") * own_blocks * MICRO_TOKENS,
        own_blocks * MICRO_TOKENS,
    ).reshape(own_blocks, MICRO_TOKENS)
    other, received, own_allowed = lax.optimization_barrier(
        (other, received, block_mask(own_segments))
    )
    pool = jnp.concatenate([got, received], axis=0)
    my_order = lax.dynamic_slice_in_dim(order, section_index * rows_here, rows_here)
    source_group = my_order // entry_rows
    within = my_order % entry_rows
    from_other = (within // part_rows) != section_index
    pool_index = (
        jnp.where(from_other, group_count * part_rows, 0)
        + source_group * part_rows
        + within % part_rows
    )
    hidden = jnp.take(pool, pool_index, axis=0)
    for layer_index in range(section_count):
        params = jax.tree.map(
            lambda mine, theirs: jnp.where(section_index == layer_index, mine, theirs), own, other
        )
        hidden = section_layer(hidden, own_allowed, *params)
    return hidden


def solution(mesh):
    placed = (
        P("dp", None),
        P(),
        P(),
        P("section", "dp"),
        P("section", "dp", "tensor"),
        P("section", "dp", "tensor", None),
        P("section", "tensor", "dp"),
    )
    return jax.shard_map(
        on_device, mesh=mesh, in_specs=placed, out_specs=P("section", "dp"), check_vma=False
    )
```

```python
import math

import jax
import jax.numpy as jnp
from jax import lax
from jax.sharding import PartitionSpec as P

MODEL_WIDTH = 16384
KEYVALUE_HEADS = 8
QUERY_HEADS = 64
MICRO_TOKENS = 32
HEAD_WIDTH = 128
SPARE_COLUMNS = 128
M = 4


norm_epsilon = 1e-05


def causal_block_attend(query_rows, key_value_rows, allowed, query_group_width):
    block_count, row_count = allowed.shape[:2]
    kv_heads = key_value_rows.shape[1]
    head_size = key_value_rows.shape[2] // 2
    query_head_rows = query_rows.reshape(
        block_count, row_count, kv_heads, query_group_width, head_size
    )
    key_value_blocks = key_value_rows.reshape(block_count, row_count, kv_heads, 2 * head_size)
    key_heads = key_value_blocks[..., :head_size]
    value_heads = key_value_blocks[..., head_size:]
    scores = jnp.einsum(
        "bqkgd,bskd->bkgqs", query_head_rows, key_heads, preferred_element_type=jnp.float32
    ) / math.sqrt(head_size)
    raw_weights = jnp.where(allowed[:, None, None], jnp.exp(scores), 0.0)
    totals = jnp.sum(raw_weights, axis=-1, keepdims=True)
    probs = (raw_weights / totals).astype(jnp.bfloat16)
    attended_rows = jnp.einsum(
        "bkgqs,bskd->bqkgd", probs, value_heads, preferred_element_type=jnp.float32
    )
    return attended_rows.astype(jnp.bfloat16).reshape(
        block_count * row_count, kv_heads * query_group_width * head_size
    )


def block_mask(sentence_segment_rows):
    row_count = sentence_segment_rows.shape[1]
    position = jnp.arange(row_count)
    return (sentence_segment_rows[:, :, None] == sentence_segment_rows[:, None, :]) & (
        position[None, :] <= position[:, None]
    )[None]


def gathered_over(block, axis):
    count = lax.axis_size(axis)
    spread = jnp.broadcast_to(block[None], (count,) + block.shape)
    return lax.all_to_all(spread, axis, 0, 0, tiled=False).reshape(
        (count * block.shape[0],) + block.shape[1:]
    )


def section_layer(hidden, own_allowed, gain_row, joined_weight, out_weight, known_rms):
    row_count = hidden.shape[0]
    group_count = lax.axis_size("dp")
    own_rows = row_count // group_count
    widened = hidden.astype(jnp.float32)
    normed_rows = (widened * gain_row[None, :]).astype(jnp.bfloat16)
    query_width = out_weight.shape[0]
    keyval_width = joined_weight.shape[1] - query_width - SPARE_COLUMNS
    square_column = query_width + keyval_width
    if known_rms is None:
        joined_terms = jnp.dot(normed_rows, joined_weight, preferred_element_type=jnp.float32)
        square_terms = jnp.sum(widened * widened, axis=1, keepdims=True)
        square_high = lax.reduce_precision(square_terms, exponent_bits=8, mantissa_bits=7)
        square_low = square_terms - square_high
        column = lax.broadcasted_iota(jnp.int32, joined_terms.shape, 1)
        payload = jnp.where(
            column == square_column,
            square_high,
            jnp.where(column == square_column + 1, square_low, joined_terms),
        ).astype(jnp.bfloat16)
    else:
        payload = jnp.dot(
            normed_rows, joined_weight[:, :square_column], preferred_element_type=jnp.float32
        ).astype(jnp.bfloat16)
    arrived = lax.all_to_all(
        payload.reshape(group_count, own_rows, payload.shape[1]), "dp", 0, 0, tiled=False
    )
    summed = jnp.sum(arrived.astype(jnp.float32), axis=0)
    if known_rms is None:
        own_squares = summed[:, square_column] + summed[:, square_column + 1]
        root_mean_square = jnp.sqrt(own_squares / MODEL_WIDTH + norm_epsilon)
    else:
        root_mean_square = known_rms
    scaled_sums = summed[:, : query_width + keyval_width] / root_mean_square[:, None]
    query_rows = scaled_sums[:, :query_width].astype(jnp.bfloat16)
    key_value_rows = (
        scaled_sums[:, query_width:]
        .astype(jnp.bfloat16)
        .reshape(own_rows, -1, 2 * HEAD_WIDTH)
    )
    attended_rows = causal_block_attend(
        query_rows, key_value_rows, own_allowed, QUERY_HEADS // KEYVALUE_HEADS
    )
    head_terms = jnp.dot(
        gathered_over(attended_rows, "dp"), out_weight, preferred_element_type=jnp.float32
    )
    head_total = lax.psum(head_terms.astype(jnp.bfloat16), "tensor").astype(jnp.float32)
    return (widened + head_total).astype(jnp.bfloat16)


def on_device(tokens, order, segments, gain, w_query, key_value_weight, w_out):
    section_count = lax.axis_size("section")
    section_index = lax.axis_index("section")
    group_count = lax.axis_size("dp")
    slice_width = w_query.shape[1]
    joined = jnp.concatenate(
        [
            w_query[0],
            key_value_weight[0].reshape(slice_width, -1),
            jnp.zeros((slice_width, SPARE_COLUMNS), w_query.dtype),
        ],
        axis=1,
    )
    own = (gain[0], joined, w_out[0])
    swap = [(i, (i + 1) % section_count) for i in range(section_count)]
    other = lax.ppermute(own, "section", swap)
    entry_rows, model_width = tokens.shape
    part_rows = entry_rows // section_count
    my_rows = lax.dynamic_slice_in_dim(tokens, section_index * part_rows, part_rows)
    got = lax.all_to_all(
        my_rows.reshape(part_rows, group_count, model_width // group_count), "dp", 1, 0, tiled=True
    ).reshape(group_count * part_rows, -1)
    received = lax.ppermute(got, "section", swap)
    rows_here = group_count * entry_rows // section_count
    own_blocks = rows_here // (group_count * MICRO_TOKENS)
    own_segments = lax.dynamic_slice_in_dim(
        segments,
        section_index * rows_here + lax.axis_index("dp") * own_blocks * MICRO_TOKENS,
        own_blocks * MICRO_TOKENS,
    ).reshape(own_blocks, MICRO_TOKENS)
    entry_squares = lax.all_gather(
        jnp.sum(jnp.square(tokens.astype(jnp.float32)), axis=1), "dp", tiled=True
    )
    own_order = lax.dynamic_slice_in_dim(
        order,
        section_index * rows_here + lax.axis_index("dp") * own_blocks * MICRO_TOKENS,
        own_blocks * MICRO_TOKENS,
    )
    other, received, own_allowed, first_rms = lax.optimization_barrier(
        (
            other,
            received,
            block_mask(own_segments),
            jnp.sqrt(jnp.take(entry_squares, own_order) / MODEL_WIDTH + norm_epsilon),
        )
    )
    pool = jnp.concatenate([got, received], axis=0)
    my_order = lax.dynamic_slice_in_dim(order, section_index * rows_here, rows_here)
    source_group = my_order // entry_rows
    within = my_order % entry_rows
    from_other = (within // part_rows) != section_index
    pool_index = (
        jnp.where(from_other, group_count * part_rows, 0)
        + source_group * part_rows
        + within % part_rows
    )
    hidden = jnp.take(pool, pool_index, axis=0)
    known_rms = first_rms
    for layer_index in range(section_count):
        params = jax.tree.map(
            lambda mine, theirs: jnp.where(section_index == layer_index, mine, theirs), own, other
        )
        hidden = section_layer(hidden, own_allowed, *params, known_rms)
        known_rms = None
    return hidden


def solution(mesh):
    placed = (
        P("dp", None),
        P(),
        P(),
        P("section", "dp"),
        P("section", "dp", "tensor"),
        P("section", "dp", "tensor", None),
        P("section", "tensor", "dp"),
    )
    return jax.shard_map(
        on_device, mesh=mesh, in_specs=placed, out_specs=P("section", "dp"), check_vma=False
    )
```

```python
import math

import jax
import jax.numpy as jnp
from jax import lax
from jax.sharding import PartitionSpec as P

MODEL_WIDTH = 16384
KEYVALUE_HEADS = 8
QUERY_HEADS = 64
MICRO_TOKENS = 32
HEAD_WIDTH = 128
SPARE_COLUMNS = 128
M = 4


norm_epsilon = 1e-05


def causal_block_attend(query_rows, key_value_rows, allowed, query_group_width):
    block_count, row_count = allowed.shape[:2]
    kv_heads = key_value_rows.shape[1]
    head_size = key_value_rows.shape[2] // 2
    query_head_rows = query_rows.reshape(
        block_count, row_count, kv_heads, query_group_width, head_size
    )
    key_value_blocks = key_value_rows.reshape(block_count, row_count, kv_heads, 2 * head_size)
    key_heads = key_value_blocks[..., :head_size]
    value_heads = key_value_blocks[..., head_size:]
    scores = jnp.einsum(
        "bqkgd,bskd->bkgqs", query_head_rows, key_heads, preferred_element_type=jnp.float32
    ) / math.sqrt(head_size)
    raw_weights = jnp.where(allowed[:, None, None], jnp.exp(scores), 0.0)
    totals = jnp.sum(raw_weights, axis=-1, keepdims=True)
    probs = (raw_weights / totals).astype(jnp.bfloat16)
    attended_rows = jnp.einsum(
        "bkgqs,bskd->bqkgd", probs, value_heads, preferred_element_type=jnp.float32
    )
    return attended_rows.astype(jnp.bfloat16).reshape(
        block_count * row_count, kv_heads * query_group_width * head_size
    )


def block_mask(sentence_segment_rows):
    row_count = sentence_segment_rows.shape[1]
    position = jnp.arange(row_count)
    return (sentence_segment_rows[:, :, None] == sentence_segment_rows[:, None, :]) & (
        position[None, :] <= position[:, None]
    )[None]


def gathered_over(block, axis):
    count = lax.axis_size(axis)
    spread = jnp.broadcast_to(block[None], (count,) + block.shape)
    return lax.all_to_all(spread, axis, 0, 0, tiled=False).reshape(
        (count * block.shape[0],) + block.shape[1:]
    )


def section_layer(hidden, own_allowed, gain_row, joined_weight, out_weight):
    row_count = hidden.shape[0]
    group_count = lax.axis_size("dp")
    own_rows = row_count // group_count
    widened = hidden.astype(jnp.float32)
    normed_rows = (widened * gain_row[None, :]).astype(jnp.bfloat16)
    joined_terms = jnp.dot(normed_rows, joined_weight, preferred_element_type=jnp.float32)
    query_width = out_weight.shape[0]
    keyval_width = joined_terms.shape[1] - query_width - SPARE_COLUMNS
    square_terms = jnp.sum(widened * widened, axis=1, keepdims=True)
    square_high = lax.reduce_precision(square_terms, exponent_bits=8, mantissa_bits=7)
    square_low = square_terms - square_high
    column = lax.broadcasted_iota(jnp.int32, joined_terms.shape, 1)
    square_column = query_width + keyval_width
    payload = jnp.where(
        column == square_column,
        square_high,
        jnp.where(column == square_column + 1, square_low, joined_terms),
    ).astype(jnp.bfloat16)
    arrived = lax.all_to_all(
        payload.reshape(group_count, own_rows, payload.shape[1]), "dp", 0, 0, tiled=False
    )
    summed = jnp.sum(arrived.astype(jnp.float32), axis=0)
    own_squares = summed[:, query_width + keyval_width] + summed[:, query_width + keyval_width + 1]
    root_mean_square = jnp.sqrt(own_squares / MODEL_WIDTH + norm_epsilon)
    scaled_sums = summed[:, : query_width + keyval_width] / root_mean_square[:, None]
    query_rows = scaled_sums[:, :query_width].astype(jnp.bfloat16)
    key_value_rows = (
        scaled_sums[:, query_width:]
        .astype(jnp.bfloat16)
        .reshape(own_rows, -1, 2 * HEAD_WIDTH)
    )
    attended_rows = causal_block_attend(
        query_rows, key_value_rows, own_allowed, QUERY_HEADS // KEYVALUE_HEADS
    )
    head_terms = jnp.dot(
        gathered_over(attended_rows, "dp"), out_weight, preferred_element_type=jnp.float32
    )
    head_total = lax.psum(head_terms.astype(jnp.bfloat16), "tensor").astype(jnp.float32)
    return (widened + head_total).astype(jnp.bfloat16)


def on_device(tokens, order, segments, gain, w_query, key_value_weight, w_out):
    section_count = lax.axis_size("section")
    section_index = lax.axis_index("section")
    group_count = lax.axis_size("dp")
    slice_width = w_query.shape[1]
    joined = jnp.concatenate(
        [
            w_query[0],
            key_value_weight[0].reshape(slice_width, -1),
            jnp.zeros((slice_width, SPARE_COLUMNS), w_query.dtype),
        ],
        axis=1,
    )
    own = (gain[0], joined, w_out[0])
    swap = [(i, (i + 1) % section_count) for i in range(section_count)]
    other = lax.ppermute(own, "section", swap)
    entry_rows, model_width = tokens.shape
    part_rows = entry_rows // section_count
    my_rows = lax.dynamic_slice_in_dim(tokens, section_index * part_rows, part_rows)
    got = lax.all_to_all(
        my_rows.reshape(part_rows, group_count, model_width // group_count), "dp", 1, 0, tiled=True
    ).reshape(group_count * part_rows, -1)
    received = lax.ppermute(got, "section", swap)
    rows_here = group_count * entry_rows // section_count
    own_blocks = rows_here // (group_count * MICRO_TOKENS)
    own_segments = lax.dynamic_slice_in_dim(
        segments,
        section_index * rows_here + lax.axis_index("dp") * own_blocks * MICRO_TOKENS,
        own_blocks * MICRO_TOKENS,
    ).reshape(own_blocks, MICRO_TOKENS)
    other, received, own_allowed = lax.optimization_barrier(
        (other, received, block_mask(own_segments))
    )
    my_order = lax.dynamic_slice_in_dim(order, section_index * rows_here, rows_here)
    source_group = my_order // entry_rows
    within = my_order % entry_rows
    from_other = (within // part_rows) != section_index
    block_index = source_group * part_rows + within % part_rows
    hits = lax.broadcasted_iota(jnp.int32, (rows_here, got.shape[0]), 1) == block_index[:, None]
    picked_here = (hits & ~from_other[:, None]).astype(got.dtype)
    picked_there = (hits & from_other[:, None]).astype(got.dtype)
    hidden = (
        jnp.dot(picked_here, got, preferred_element_type=jnp.float32)
        + jnp.dot(picked_there, received, preferred_element_type=jnp.float32)
    ).astype(got.dtype)
    for layer_index in range(section_count):
        params = jax.tree.map(
            lambda mine, theirs: jnp.where(section_index == layer_index, mine, theirs), own, other
        )
        hidden = section_layer(hidden, own_allowed, *params)
    return hidden


def solution(mesh):
    placed = (
        P("dp", None),
        P(),
        P(),
        P("section", "dp"),
        P("section", "dp", "tensor"),
        P("section", "dp", "tensor", None),
        P("section", "tensor", "dp"),
    )
    return jax.shard_map(
        on_device, mesh=mesh, in_specs=placed, out_specs=P("section", "dp"), check_vma=False
    )
```

```python
import math

import jax
import jax.numpy as jnp
from jax import lax
from jax.sharding import PartitionSpec as P

MODEL_WIDTH = 16384
KEYVALUE_HEADS = 8
QUERY_HEADS = 64
MICRO_TOKENS = 32
HEAD_WIDTH = 128
SPARE_COLUMNS = 128
M = 4


norm_epsilon = 1e-05


def causal_block_attend(query_rows, key_value_rows, allowed, query_group_width):
    block_count, row_count = allowed.shape[:2]
    kv_heads = key_value_rows.shape[1]
    head_size = key_value_rows.shape[2] // 2
    query_head_rows = query_rows.reshape(
        block_count, row_count, kv_heads, query_group_width, head_size
    )
    key_value_blocks = key_value_rows.reshape(block_count, row_count, kv_heads, 2 * head_size)
    key_heads = key_value_blocks[..., :head_size]
    value_heads = key_value_blocks[..., head_size:]
    scores = jnp.einsum(
        "bqkgd,bskd->bkgqs", query_head_rows, key_heads, preferred_element_type=jnp.float32
    ) / math.sqrt(head_size)
    raw_weights = jnp.where(allowed[:, None, None], jnp.exp(scores), 0.0)
    totals = jnp.sum(raw_weights, axis=-1, keepdims=True)
    probs = (raw_weights / totals).astype(jnp.bfloat16)
    attended_rows = jnp.einsum(
        "bkgqs,bskd->bqkgd", probs, value_heads, preferred_element_type=jnp.float32
    )
    return attended_rows.astype(jnp.bfloat16).reshape(
        block_count * row_count, kv_heads * query_group_width * head_size
    )


def block_mask(sentence_segment_rows):
    row_count = sentence_segment_rows.shape[1]
    position = jnp.arange(row_count)
    return (sentence_segment_rows[:, :, None] == sentence_segment_rows[:, None, :]) & (
        position[None, :] <= position[:, None]
    )[None]


def gathered_over(block, axis):
    count = lax.axis_size(axis)
    spread = jnp.broadcast_to(block[None], (count,) + block.shape)
    return lax.all_to_all(spread, axis, 0, 0, tiled=False).reshape(
        (count * block.shape[0],) + block.shape[1:]
    )


def section_layer(hidden, own_allowed, gain_row, joined_weight, out_weight):
    row_count = hidden.shape[0]
    group_count = lax.axis_size("dp")
    own_rows = row_count // group_count
    widened = hidden.astype(jnp.float32)
    normed_rows = (widened * gain_row[None, :]).astype(jnp.bfloat16)
    joined_terms = jnp.dot(normed_rows, joined_weight, preferred_element_type=jnp.float32)
    query_width = out_weight.shape[0]
    keyval_width = joined_terms.shape[1] - query_width - SPARE_COLUMNS
    square_terms = jnp.sum(widened * widened, axis=1, keepdims=True)
    square_high = lax.reduce_precision(square_terms, exponent_bits=8, mantissa_bits=7)
    square_low = square_terms - square_high
    column = lax.broadcasted_iota(jnp.int32, joined_terms.shape, 1)
    square_column = query_width + keyval_width
    payload = jnp.where(
        column == square_column,
        square_high,
        jnp.where(column == square_column + 1, square_low, joined_terms),
    ).astype(jnp.bfloat16)
    arrived = lax.all_to_all(
        payload.reshape(group_count, own_rows, payload.shape[1]), "dp", 0, 0, tiled=False
    )
    summed = jnp.sum(arrived.astype(jnp.float32), axis=0)
    own_squares = summed[:, query_width + keyval_width] + summed[:, query_width + keyval_width + 1]
    root_mean_square = jnp.sqrt(own_squares / MODEL_WIDTH + norm_epsilon)
    scaled_sums = summed[:, : query_width + keyval_width] / root_mean_square[:, None]
    query_rows = scaled_sums[:, :query_width].astype(jnp.bfloat16)
    key_value_rows = (
        scaled_sums[:, query_width:]
        .astype(jnp.bfloat16)
        .reshape(own_rows, -1, 2 * HEAD_WIDTH)
    )
    attended_rows = causal_block_attend(
        query_rows, key_value_rows, own_allowed, QUERY_HEADS // KEYVALUE_HEADS
    )
    all_attended = gathered_over(attended_rows, "dp")
    split_at = out_weight.shape[1] // 2
    engine_sum = lax.psum(
        jnp.dot(
            all_attended, out_weight[:, :split_at], preferred_element_type=jnp.float32
        ).astype(jnp.bfloat16),
        "tensor",
    )
    core_terms = jnp.dot(
        all_attended, out_weight[:, split_at:], preferred_element_type=jnp.float32
    ).astype(jnp.bfloat16)
    tensor_count = lax.axis_size("tensor")
    core_pieces = lax.all_to_all(
        core_terms.reshape(tensor_count, row_count // tensor_count, -1),
        "tensor",
        0,
        0,
        tiled=False,
    )
    core_sum = gathered_over(
        jnp.sum(core_pieces.astype(jnp.float32), axis=0).astype(jnp.bfloat16), "tensor"
    )
    head_total = jnp.concatenate([engine_sum, core_sum], axis=1).astype(jnp.float32)
    return (widened + head_total).astype(jnp.bfloat16)


def on_device(tokens, order, segments, gain, w_query, key_value_weight, w_out):
    section_count = lax.axis_size("section")
    section_index = lax.axis_index("section")
    group_count = lax.axis_size("dp")
    slice_width = w_query.shape[1]
    joined = jnp.concatenate(
        [
            w_query[0],
            key_value_weight[0].reshape(slice_width, -1),
            jnp.zeros((slice_width, SPARE_COLUMNS), w_query.dtype),
        ],
        axis=1,
    )
    own = (gain[0], joined, w_out[0])
    swap = [(i, (i + 1) % section_count) for i in range(section_count)]
    other = lax.ppermute(own, "section", swap)
    entry_rows, model_width = tokens.shape
    part_rows = entry_rows // section_count
    my_rows = lax.dynamic_slice_in_dim(tokens, section_index * part_rows, part_rows)
    got = lax.all_to_all(
        my_rows.reshape(part_rows, group_count, model_width // group_count), "dp", 1, 0, tiled=True
    ).reshape(group_count * part_rows, -1)
    received = lax.ppermute(got, "section", swap)
    rows_here = group_count * entry_rows // section_count
    own_blocks = rows_here // (group_count * MICRO_TOKENS)
    own_segments = lax.dynamic_slice_in_dim(
        segments,
        section_index * rows_here + lax.axis_index("dp") * own_blocks * MICRO_TOKENS,
        own_blocks * MICRO_TOKENS,
    ).reshape(own_blocks, MICRO_TOKENS)
    other, received, own_allowed = lax.optimization_barrier(
        (other, received, block_mask(own_segments))
    )
    pool = jnp.concatenate([got, received], axis=0)
    my_order = lax.dynamic_slice_in_dim(order, section_index * rows_here, rows_here)
    source_group = my_order // entry_rows
    within = my_order % entry_rows
    from_other = (within // part_rows) != section_index
    pool_index = (
        jnp.where(from_other, group_count * part_rows, 0)
        + source_group * part_rows
        + within % part_rows
    )
    hidden = jnp.take(pool, pool_index, axis=0)
    for layer_index in range(section_count):
        params = jax.tree.map(
            lambda mine, theirs: jnp.where(section_index == layer_index, mine, theirs), own, other
        )
        hidden = section_layer(hidden, own_allowed, *params)
    return hidden


def solution(mesh):
    placed = (
        P("dp", None),
        P(),
        P(),
        P("section", "dp"),
        P("section", "dp", "tensor"),
        P("section", "dp", "tensor", None),
        P("section", "tensor", "dp"),
    )
    return jax.shard_map(
        on_device, mesh=mesh, in_specs=placed, out_specs=P("section", "dp"), check_vma=False
    )
```

```python
import math

import jax
import jax.numpy as jnp
from jax import lax
from jax.experimental.layout import Layout, with_layout_constraint
from jax.sharding import PartitionSpec as P

MODEL_WIDTH = 16384
KEYVALUE_HEADS = 8
QUERY_HEADS = 64
MICRO_TOKENS = 32
HEAD_WIDTH = 128
SPARE_COLUMNS = 128
M = 4


norm_epsilon = 1e-05


def causal_block_attend(query_rows, key_value_rows, allowed, query_group_width):
    block_count, row_count = allowed.shape[:2]
    kv_heads = key_value_rows.shape[1]
    head_size = key_value_rows.shape[2] // 2
    query_head_rows = query_rows.reshape(
        block_count, row_count, kv_heads, query_group_width, head_size
    )
    key_value_blocks = key_value_rows.reshape(block_count, row_count, kv_heads, 2 * head_size)
    key_heads = key_value_blocks[..., :head_size]
    value_heads = key_value_blocks[..., head_size:]
    scores = jnp.einsum(
        "bqkgd,bskd->bkgqs", query_head_rows, key_heads, preferred_element_type=jnp.float32
    ) / math.sqrt(head_size)
    raw_weights = jnp.where(allowed[:, None, None], jnp.exp(scores), 0.0)
    totals = jnp.sum(raw_weights, axis=-1, keepdims=True)
    probs = (raw_weights / totals).astype(jnp.bfloat16)
    attended_rows = jnp.einsum(
        "bkgqs,bskd->bqkgd", probs, value_heads, preferred_element_type=jnp.float32
    )
    return attended_rows.astype(jnp.bfloat16).reshape(
        block_count * row_count, kv_heads * query_group_width * head_size
    )


def block_mask(sentence_segment_rows):
    row_count = sentence_segment_rows.shape[1]
    position = jnp.arange(row_count)
    return (sentence_segment_rows[:, :, None] == sentence_segment_rows[:, None, :]) & (
        position[None, :] <= position[:, None]
    )[None]


def gathered_over(block, axis):
    count = lax.axis_size(axis)
    spread = jnp.broadcast_to(block[None], (count,) + block.shape)
    return lax.all_to_all(spread, axis, 0, 0, tiled=False).reshape(
        (count * block.shape[0],) + block.shape[1:]
    )


def section_layer(hidden, own_allowed, gain_row, joined_weight, out_weight):
    row_count = hidden.shape[0]
    group_count = lax.axis_size("dp")
    own_rows = row_count // group_count
    widened = hidden.astype(jnp.float32)
    normed_rows = (widened * gain_row[None, :]).astype(jnp.bfloat16)
    joined_terms = jnp.dot(normed_rows, joined_weight, preferred_element_type=jnp.float32)
    query_width = out_weight.shape[0]
    keyval_width = joined_terms.shape[1] - query_width - SPARE_COLUMNS
    square_terms = jnp.sum(widened * widened, axis=1, keepdims=True)
    square_high = lax.reduce_precision(square_terms, exponent_bits=8, mantissa_bits=7)
    square_low = square_terms - square_high
    column = lax.broadcasted_iota(jnp.int32, joined_terms.shape, 1)
    square_column = query_width + keyval_width
    payload = jnp.where(
        column == square_column,
        square_high,
        jnp.where(column == square_column + 1, square_low, joined_terms),
    ).astype(jnp.bfloat16)
    arrived = lax.all_to_all(
        payload.reshape(group_count, own_rows, payload.shape[1]), "dp", 0, 0, tiled=False
    )
    summed = jnp.sum(arrived.astype(jnp.float32), axis=0)
    own_squares = summed[:, query_width + keyval_width] + summed[:, query_width + keyval_width + 1]
    root_mean_square = jnp.sqrt(own_squares / MODEL_WIDTH + norm_epsilon)
    scaled_sums = summed[:, : query_width + keyval_width] / root_mean_square[:, None]
    query_rows = scaled_sums[:, :query_width].astype(jnp.bfloat16)
    key_value_rows = (
        scaled_sums[:, query_width:]
        .astype(jnp.bfloat16)
        .reshape(own_rows, -1, 2 * HEAD_WIDTH)
    )
    attended_rows = causal_block_attend(
        query_rows, key_value_rows, own_allowed, QUERY_HEADS // KEYVALUE_HEADS
    )
    head_terms = jnp.dot(
        gathered_over(attended_rows, "dp"), out_weight, preferred_element_type=jnp.float32
    )
    head_total = lax.psum(head_terms.astype(jnp.bfloat16), "tensor").astype(jnp.float32)
    return (widened + head_total).astype(jnp.bfloat16)


def on_device(tokens, order, segments, gain, w_query, key_value_weight, w_out):
    section_count = lax.axis_size("section")
    section_index = lax.axis_index("section")
    group_count = lax.axis_size("dp")
    slice_width = w_query.shape[1]
    joined = jnp.concatenate(
        [
            w_query[0],
            key_value_weight[0].reshape(slice_width, -1),
            jnp.zeros((slice_width, SPARE_COLUMNS), w_query.dtype),
        ],
        axis=1,
    )
    own = (gain[0], joined, w_out[0])
    swap = [(i, (i + 1) % section_count) for i in range(section_count)]
    other = lax.ppermute(own, "section", swap)
    entry_rows, model_width = tokens.shape
    part_rows = entry_rows // section_count
    my_rows = lax.dynamic_slice_in_dim(tokens, section_index * part_rows, part_rows)
    got = lax.all_to_all(
        my_rows.reshape(part_rows, group_count, model_width // group_count), "dp", 1, 0, tiled=True
    ).reshape(group_count * part_rows, -1)
    received = lax.ppermute(got, "section", swap)
    rows_here = group_count * entry_rows // section_count
    own_blocks = rows_here // (group_count * MICRO_TOKENS)
    own_segments = lax.dynamic_slice_in_dim(
        segments,
        section_index * rows_here + lax.axis_index("dp") * own_blocks * MICRO_TOKENS,
        own_blocks * MICRO_TOKENS,
    ).reshape(own_blocks, MICRO_TOKENS)
    other, received, own_allowed = lax.optimization_barrier(
        (other, received, block_mask(own_segments))
    )
    my_order = lax.dynamic_slice_in_dim(order, section_index * rows_here, rows_here)
    source_group = my_order // entry_rows
    within = my_order % entry_rows
    from_other = (within // part_rows) != section_index
    block_index = source_group * part_rows + within % part_rows
    hits = lax.broadcasted_iota(jnp.int32, (rows_here, got.shape[0]), 1) == block_index[:, None]
    picked_here = (hits & ~from_other[:, None]).astype(got.dtype)
    picked_there = (hits & from_other[:, None]).astype(got.dtype)
    hidden = (
        jnp.dot(picked_here, got, preferred_element_type=jnp.float32)
        + jnp.dot(picked_there, received, preferred_element_type=jnp.float32)
    ).astype(got.dtype)
    hidden = with_layout_constraint(hidden, Layout(major_to_minor=(0, 1)))
    for layer_index in range(section_count):
        params = jax.tree.map(
            lambda mine, theirs: jnp.where(section_index == layer_index, mine, theirs), own, other
        )
        hidden = section_layer(hidden, own_allowed, *params)
    return hidden


def solution(mesh):
    placed = (
        P("dp", None),
        P(),
        P(),
        P("section", "dp"),
        P("section", "dp", "tensor"),
        P("section", "dp", "tensor", None),
        P("section", "tensor", "dp"),
    )
    return jax.shard_map(
        on_device, mesh=mesh, in_specs=placed, out_specs=P("section", "dp"), check_vma=False
    )
```

```python
import math

import jax
import jax.numpy as jnp
from jax import lax
from jax.experimental.layout import Layout, with_layout_constraint
from jax.sharding import PartitionSpec as P

MODEL_WIDTH = 16384
KEYVALUE_HEADS = 8
QUERY_HEADS = 64
MICRO_TOKENS = 32
HEAD_WIDTH = 128
SPARE_COLUMNS = 128
M = 4


norm_epsilon = 1e-05


def causal_block_attend(query_rows, key_value_rows, allowed, query_group_width):
    block_count, row_count = allowed.shape[:2]
    kv_heads = key_value_rows.shape[1]
    head_size = key_value_rows.shape[2] // 2
    query_head_rows = query_rows.reshape(
        block_count, row_count, kv_heads, query_group_width, head_size
    )
    key_value_blocks = key_value_rows.reshape(block_count, row_count, kv_heads, 2 * head_size)
    key_heads = key_value_blocks[..., :head_size]
    value_heads = key_value_blocks[..., head_size:]
    scores = jnp.einsum(
        "bqkgd,bskd->bkgqs", query_head_rows, key_heads, preferred_element_type=jnp.float32
    ) / math.sqrt(head_size)
    raw_weights = jnp.where(allowed[:, None, None], jnp.exp(scores), 0.0)
    totals = jnp.sum(raw_weights, axis=-1, keepdims=True)
    probs = (raw_weights / totals).astype(jnp.bfloat16)
    attended_rows = jnp.einsum(
        "bkgqs,bskd->bqkgd", probs, value_heads, preferred_element_type=jnp.float32
    )
    return attended_rows.astype(jnp.bfloat16).reshape(
        block_count * row_count, kv_heads * query_group_width * head_size
    )


def block_mask(sentence_segment_rows):
    row_count = sentence_segment_rows.shape[1]
    position = jnp.arange(row_count)
    return (sentence_segment_rows[:, :, None] == sentence_segment_rows[:, None, :]) & (
        position[None, :] <= position[:, None]
    )[None]


def gathered_over(block, axis):
    count = lax.axis_size(axis)
    spread = jnp.broadcast_to(block[None], (count,) + block.shape)
    return lax.all_to_all(spread, axis, 0, 0, tiled=False).reshape(
        (count * block.shape[0],) + block.shape[1:]
    )


def section_layer(hidden, own_allowed, gain_row, joined_weight, out_weight):
    row_count = hidden.shape[0]
    group_count = lax.axis_size("dp")
    own_rows = row_count // group_count
    widened = hidden.astype(jnp.float32)
    normed_rows = (widened * gain_row[None, :]).astype(jnp.bfloat16)
    joined_terms = jnp.dot(normed_rows, joined_weight, preferred_element_type=jnp.float32)
    query_width = out_weight.shape[0]
    keyval_width = joined_terms.shape[1] - query_width - SPARE_COLUMNS
    square_terms = jnp.sum(widened * widened, axis=1, keepdims=True)
    square_high = lax.reduce_precision(square_terms, exponent_bits=8, mantissa_bits=7)
    square_low = square_terms - square_high
    column = lax.broadcasted_iota(jnp.int32, joined_terms.shape, 1)
    square_column = query_width + keyval_width
    payload = jnp.where(
        column == square_column,
        square_high,
        jnp.where(column == square_column + 1, square_low, joined_terms),
    ).astype(jnp.bfloat16)
    arrived = lax.all_to_all(
        payload.reshape(group_count, own_rows, payload.shape[1]), "dp", 0, 0, tiled=False
    )
    summed = jnp.sum(arrived.astype(jnp.float32), axis=0)
    own_squares = summed[:, query_width + keyval_width] + summed[:, query_width + keyval_width + 1]
    root_mean_square = jnp.sqrt(own_squares / MODEL_WIDTH + norm_epsilon)
    scaled_sums = summed[:, : query_width + keyval_width] / root_mean_square[:, None]
    query_rows = scaled_sums[:, :query_width].astype(jnp.bfloat16)
    key_value_rows = (
        scaled_sums[:, query_width:]
        .astype(jnp.bfloat16)
        .reshape(own_rows, -1, 2 * HEAD_WIDTH)
    )
    attended_rows = causal_block_attend(
        query_rows, key_value_rows, own_allowed, QUERY_HEADS // KEYVALUE_HEADS
    )
    head_terms = jnp.dot(
        gathered_over(attended_rows, "dp"), out_weight, preferred_element_type=jnp.float32
    )
    head_total = lax.psum(head_terms.astype(jnp.bfloat16), "tensor").astype(jnp.float32)
    return (widened + head_total).astype(jnp.bfloat16)


def on_device(tokens, order, segments, gain, w_query, key_value_weight, w_out):
    section_count = lax.axis_size("section")
    section_index = lax.axis_index("section")
    group_count = lax.axis_size("dp")
    slice_width = w_query.shape[1]
    joined = jnp.concatenate(
        [
            w_query[0],
            key_value_weight[0].reshape(slice_width, -1),
            jnp.zeros((slice_width, SPARE_COLUMNS), w_query.dtype),
        ],
        axis=1,
    )
    own = (gain[0], joined, w_out[0])
    swap = [(i, (i + 1) % section_count) for i in range(section_count)]
    other = lax.ppermute(own, "section", swap)
    entry_rows, model_width = tokens.shape
    part_rows = entry_rows // section_count
    my_rows = lax.dynamic_slice_in_dim(tokens, section_index * part_rows, part_rows)
    got = lax.all_to_all(
        my_rows.reshape(part_rows, group_count, model_width // group_count), "dp", 1, 0, tiled=True
    ).reshape(group_count * part_rows, -1)
    received = lax.ppermute(got, "section", swap)
    rows_here = group_count * entry_rows // section_count
    own_blocks = rows_here // (group_count * MICRO_TOKENS)
    own_segments = lax.dynamic_slice_in_dim(
        segments,
        section_index * rows_here + lax.axis_index("dp") * own_blocks * MICRO_TOKENS,
        own_blocks * MICRO_TOKENS,
    ).reshape(own_blocks, MICRO_TOKENS)
    other, received, own_allowed = lax.optimization_barrier(
        (other, received, block_mask(own_segments))
    )
    my_order = lax.dynamic_slice_in_dim(order, section_index * rows_here, rows_here)
    source_group = my_order // entry_rows
    within = my_order % entry_rows
    from_other = (within // part_rows) != section_index
    block_index = source_group * part_rows + within % part_rows
    hits = lax.broadcasted_iota(jnp.int32, (rows_here, got.shape[0]), 1) == block_index[:, None]
    picked_here = (hits & ~from_other[:, None]).astype(got.dtype)
    picked_there = (hits & from_other[:, None]).astype(got.dtype)
    hidden = (
        jnp.dot(picked_here, got, preferred_element_type=jnp.float32)
        + jnp.dot(picked_there, received, preferred_element_type=jnp.float32)
    ).astype(got.dtype)
    hidden = with_layout_constraint(hidden, Layout(major_to_minor=(0, 1)))
    for layer_index in range(section_count):
        params = jax.tree.map(
            lambda mine, theirs: jnp.where(section_index == layer_index, mine, theirs), own, other
        )
        hidden = lax.optimization_barrier(section_layer(hidden, own_allowed, *params))
    return hidden


def solution(mesh):
    placed = (
        P("dp", None),
        P(),
        P(),
        P("section", "dp"),
        P("section", "dp", "tensor"),
        P("section", "dp", "tensor", None),
        P("section", "tensor", "dp"),
    )
    return jax.shard_map(
        on_device, mesh=mesh, in_specs=placed, out_specs=P("section", "dp"), check_vma=False
    )
```

```python
import math

import jax
import jax.numpy as jnp
from jax import lax
from jax.experimental.layout import Layout, with_layout_constraint
from jax.sharding import PartitionSpec as P

MODEL_WIDTH = 16384
KEYVALUE_HEADS = 8
QUERY_HEADS = 64
MICRO_TOKENS = 32
HEAD_WIDTH = 128
SPARE_COLUMNS = 128
M = 4


norm_epsilon = 1e-05


def causal_block_attend(query_rows, key_value_rows, allowed, query_group_width):
    block_count, row_count = allowed.shape[:2]
    kv_heads = key_value_rows.shape[1]
    head_size = key_value_rows.shape[2] // 2
    query_head_rows = query_rows.reshape(
        block_count, row_count, kv_heads, query_group_width, head_size
    )
    key_value_blocks = key_value_rows.reshape(block_count, row_count, kv_heads, 2 * head_size)
    key_heads = key_value_blocks[..., :head_size]
    value_heads = key_value_blocks[..., head_size:]
    scores = jnp.einsum(
        "bqkgd,bskd->bkgqs", query_head_rows, key_heads, preferred_element_type=jnp.float32
    ) / math.sqrt(head_size)
    raw_weights = jnp.where(allowed[:, None, None], jnp.exp(scores), 0.0)
    totals = jnp.sum(raw_weights, axis=-1, keepdims=True)
    probs = (raw_weights / totals).astype(jnp.bfloat16)
    attended_rows = jnp.einsum(
        "bkgqs,bskd->bqkgd", probs, value_heads, preferred_element_type=jnp.float32
    )
    return attended_rows.astype(jnp.bfloat16).reshape(
        block_count * row_count, kv_heads * query_group_width * head_size
    )


def block_mask(sentence_segment_rows):
    row_count = sentence_segment_rows.shape[1]
    position = jnp.arange(row_count)
    return (sentence_segment_rows[:, :, None] == sentence_segment_rows[:, None, :]) & (
        position[None, :] <= position[:, None]
    )[None]


def gathered_over(block, axis):
    count = lax.axis_size(axis)
    spread = jnp.broadcast_to(block[None], (count,) + block.shape)
    return lax.all_to_all(spread, axis, 0, 0, tiled=False).reshape(
        (count * block.shape[0],) + block.shape[1:]
    )


def section_layer(hidden, own_allowed, gain_row, joined_weight, out_weight):
    row_count = hidden.shape[0]
    group_count = lax.axis_size("dp")
    own_rows = row_count // group_count
    widened = hidden.astype(jnp.float32)
    normed_rows = (widened * gain_row[None, :]).astype(jnp.bfloat16)
    joined_terms = jnp.dot(normed_rows, joined_weight, preferred_element_type=jnp.float32)
    query_width = out_weight.shape[0]
    keyval_width = joined_terms.shape[1] - query_width - SPARE_COLUMNS
    square_terms = jnp.sum(widened * widened, axis=1, keepdims=True)
    square_high = lax.reduce_precision(square_terms, exponent_bits=8, mantissa_bits=7)
    square_low = square_terms - square_high
    column = lax.broadcasted_iota(jnp.int32, joined_terms.shape, 1)
    square_column = query_width + keyval_width
    payload = jnp.where(
        column == square_column,
        square_high,
        jnp.where(column == square_column + 1, square_low, joined_terms),
    ).astype(jnp.bfloat16)
    arrived = lax.all_to_all(
        payload.reshape(group_count, own_rows, payload.shape[1]), "dp", 0, 0, tiled=False
    )
    summed = jnp.sum(arrived.astype(jnp.float32), axis=0)
    own_squares = summed[:, query_width + keyval_width] + summed[:, query_width + keyval_width + 1]
    root_mean_square = jnp.sqrt(own_squares / MODEL_WIDTH + norm_epsilon)
    scaled_sums = summed[:, : query_width + keyval_width] / root_mean_square[:, None]
    query_rows = scaled_sums[:, :query_width].astype(jnp.bfloat16)
    key_value_rows = (
        scaled_sums[:, query_width:]
        .astype(jnp.bfloat16)
        .reshape(own_rows, -1, 2 * HEAD_WIDTH)
    )
    attended_rows = causal_block_attend(
        query_rows, key_value_rows, own_allowed, QUERY_HEADS // KEYVALUE_HEADS
    )
    head_terms = jnp.dot(
        gathered_over(attended_rows, "dp"), out_weight, preferred_element_type=jnp.float32
    )
    head_total = lax.psum(head_terms.astype(jnp.bfloat16), "tensor").astype(jnp.float32)
    return (widened + head_total).astype(jnp.bfloat16)


def on_device(tokens, order, segments, gain, w_query, key_value_weight, w_out):
    section_count = lax.axis_size("section")
    section_index = lax.axis_index("section")
    group_count = lax.axis_size("dp")
    slice_width = w_query.shape[1]
    joined = jnp.concatenate(
        [
            w_query[0],
            key_value_weight[0].reshape(slice_width, -1),
            jnp.zeros((slice_width, SPARE_COLUMNS), w_query.dtype),
        ],
        axis=1,
    )
    own = (gain[0], joined, w_out[0])
    swap = [(i, (i + 1) % section_count) for i in range(section_count)]
    other = lax.ppermute(own, "section", swap)
    entry_rows, model_width = tokens.shape
    part_rows = entry_rows // section_count
    my_rows = lax.dynamic_slice_in_dim(tokens, section_index * part_rows, part_rows)
    got = lax.all_to_all(
        my_rows.reshape(part_rows, group_count, model_width // group_count), "dp", 1, 0, tiled=True
    ).reshape(group_count * part_rows, -1)
    received = lax.ppermute(got, "section", swap)
    rows_here = group_count * entry_rows // section_count
    own_blocks = rows_here // (group_count * MICRO_TOKENS)
    own_segments = lax.dynamic_slice_in_dim(
        segments,
        section_index * rows_here + lax.axis_index("dp") * own_blocks * MICRO_TOKENS,
        own_blocks * MICRO_TOKENS,
    ).reshape(own_blocks, MICRO_TOKENS)
    my_order = lax.dynamic_slice_in_dim(order, section_index * rows_here, rows_here)
    source_group = my_order // entry_rows
    within = my_order % entry_rows
    from_other = (within // part_rows) != section_index
    block_index = source_group * part_rows + within % part_rows
    hits = lax.broadcasted_iota(jnp.int32, (rows_here, got.shape[0]), 1) == block_index[:, None]
    other, received, own_allowed, picked_here, picked_there = lax.optimization_barrier(
        (
            other,
            received,
            block_mask(own_segments),
            (hits & ~from_other[:, None]).astype(got.dtype),
            (hits & from_other[:, None]).astype(got.dtype),
        )
    )
    hidden = (
        jnp.dot(picked_here, got, preferred_element_type=jnp.float32)
        + jnp.dot(picked_there, received, preferred_element_type=jnp.float32)
    ).astype(got.dtype)
    hidden = with_layout_constraint(hidden, Layout(major_to_minor=(0, 1)))
    for layer_index in range(section_count):
        params = jax.tree.map(
            lambda mine, theirs: jnp.where(section_index == layer_index, mine, theirs), own, other
        )
        hidden = section_layer(hidden, own_allowed, *params)
    return hidden


def solution(mesh):
    placed = (
        P("dp", None),
        P(),
        P(),
        P("section", "dp"),
        P("section", "dp", "tensor"),
        P("section", "dp", "tensor", None),
        P("section", "tensor", "dp"),
    )
    return jax.shard_map(
        on_device, mesh=mesh, in_specs=placed, out_specs=P("section", "dp"), check_vma=False
    )
```

```python
import math

import jax
import jax.numpy as jnp
from jax import lax
from jax.experimental.layout import Layout, with_layout_constraint
from jax.sharding import PartitionSpec as P

MODEL_WIDTH = 16384
KEYVALUE_HEADS = 8
QUERY_HEADS = 64
MICRO_TOKENS = 32
HEAD_WIDTH = 128
SPARE_COLUMNS = 128
M = 4


norm_epsilon = 1e-05


def causal_block_attend(query_rows, key_value_rows, allowed, query_group_width):
    block_count, row_count = allowed.shape[:2]
    kv_heads = key_value_rows.shape[1]
    head_size = key_value_rows.shape[2] // 2
    query_head_rows = query_rows.reshape(
        block_count, row_count, kv_heads, query_group_width, head_size
    )
    key_value_blocks = key_value_rows.reshape(block_count, row_count, kv_heads, 2 * head_size)
    key_heads = key_value_blocks[..., :head_size]
    value_heads = key_value_blocks[..., head_size:]
    scores = jnp.einsum(
        "bqkgd,bskd->bkgqs", query_head_rows, key_heads, preferred_element_type=jnp.float32
    ) / math.sqrt(head_size)
    raw_weights = jnp.where(allowed[:, None, None], jnp.exp(scores), 0.0)
    totals = jnp.sum(raw_weights, axis=-1, keepdims=True)
    probs = (raw_weights / totals).astype(jnp.bfloat16)
    attended_rows = jnp.einsum(
        "bkgqs,bskd->bqkgd", probs, value_heads, preferred_element_type=jnp.float32
    )
    return attended_rows.astype(jnp.bfloat16).reshape(
        block_count * row_count, kv_heads * query_group_width * head_size
    )


def block_mask(sentence_segment_rows):
    row_count = sentence_segment_rows.shape[1]
    position = jnp.arange(row_count)
    return (sentence_segment_rows[:, :, None] == sentence_segment_rows[:, None, :]) & (
        position[None, :] <= position[:, None]
    )[None]


def gathered_over(block, axis):
    count = lax.axis_size(axis)
    spread = jnp.broadcast_to(block[None], (count,) + block.shape)
    return lax.all_to_all(spread, axis, 0, 0, tiled=False).reshape(
        (count * block.shape[0],) + block.shape[1:]
    )


def section_layer(hidden, own_allowed, gain_row, joined_weight, out_weight):
    row_count = hidden.shape[0]
    group_count = lax.axis_size("dp")
    own_rows = row_count // group_count
    widened = hidden.astype(jnp.float32)
    normed_rows = (widened * gain_row[None, :]).astype(jnp.bfloat16)
    joined_terms = jnp.dot(normed_rows, joined_weight, preferred_element_type=jnp.float32)
    query_width = out_weight.shape[0]
    keyval_width = joined_terms.shape[1] - query_width - SPARE_COLUMNS
    square_terms = jnp.sum(widened * widened, axis=1, keepdims=True)
    square_high = lax.reduce_precision(square_terms, exponent_bits=8, mantissa_bits=7)
    square_low = square_terms - square_high
    column = lax.broadcasted_iota(jnp.int32, joined_terms.shape, 1)
    square_column = query_width + keyval_width
    payload = jnp.where(
        column == square_column,
        square_high,
        jnp.where(column == square_column + 1, square_low, joined_terms),
    ).astype(jnp.bfloat16)
    arrived = lax.all_to_all(
        payload.reshape(group_count, own_rows, payload.shape[1]), "dp", 0, 0, tiled=False
    )
    summed = jnp.sum(arrived.astype(jnp.float32), axis=0)
    own_squares = summed[:, query_width + keyval_width] + summed[:, query_width + keyval_width + 1]
    root_mean_square = jnp.sqrt(own_squares / MODEL_WIDTH + norm_epsilon)
    scaled_sums = summed[:, : query_width + keyval_width] / root_mean_square[:, None]
    query_rows = scaled_sums[:, :query_width].astype(jnp.bfloat16)
    key_value_rows = (
        scaled_sums[:, query_width:]
        .astype(jnp.bfloat16)
        .reshape(own_rows, -1, 2 * HEAD_WIDTH)
    )
    attended_rows = causal_block_attend(
        query_rows, key_value_rows, own_allowed, QUERY_HEADS // KEYVALUE_HEADS
    )
    head_terms = jnp.dot(
        gathered_over(attended_rows, "dp"), out_weight, preferred_element_type=jnp.float32
    )
    head_total = lax.psum(head_terms.astype(jnp.bfloat16), "tensor").astype(jnp.float32)
    return (widened + head_total).astype(jnp.bfloat16)


def on_device(tokens, order, segments, gain, w_query, key_value_weight, w_out):
    section_count = lax.axis_size("section")
    section_index = lax.axis_index("section")
    group_count = lax.axis_size("dp")
    slice_width = w_query.shape[1]
    joined = jnp.concatenate(
        [
            w_query[0],
            key_value_weight[0].reshape(slice_width, -1),
            jnp.zeros((slice_width, SPARE_COLUMNS), w_query.dtype),
        ],
        axis=1,
    )
    own = (gain[0], joined, w_out[0])
    swap = [(i, (i + 1) % section_count) for i in range(section_count)]
    other = lax.ppermute(own, "section", swap)
    entry_rows, model_width = tokens.shape
    part_rows = entry_rows // section_count
    my_rows = lax.dynamic_slice_in_dim(tokens, section_index * part_rows, part_rows)
    got = lax.all_to_all(
        my_rows.reshape(part_rows, group_count, model_width // group_count), "dp", 1, 0, tiled=True
    ).reshape(group_count * part_rows, -1)
    received = lax.ppermute(got, "section", swap)
    rows_here = group_count * entry_rows // section_count
    own_blocks = rows_here // (group_count * MICRO_TOKENS)
    own_segments = lax.dynamic_slice_in_dim(
        segments,
        section_index * rows_here + lax.axis_index("dp") * own_blocks * MICRO_TOKENS,
        own_blocks * MICRO_TOKENS,
    ).reshape(own_blocks, MICRO_TOKENS)
    other, own_allowed = lax.optimization_barrier((other, block_mask(own_segments)))
    my_order = lax.dynamic_slice_in_dim(order, section_index * rows_here, rows_here)
    source_group = my_order // entry_rows
    within = my_order % entry_rows
    from_other = (within // part_rows) != section_index
    block_index = source_group * part_rows + within % part_rows
    hits = lax.broadcasted_iota(jnp.int32, (rows_here, got.shape[0]), 1) == block_index[:, None]
    picked_here = (hits & ~from_other[:, None]).astype(got.dtype)
    picked_there = (hits & from_other[:, None]).astype(got.dtype)
    hidden = (
        jnp.dot(picked_here, got, preferred_element_type=jnp.float32)
        + jnp.dot(picked_there, received, preferred_element_type=jnp.float32)
    ).astype(got.dtype)
    hidden = with_layout_constraint(hidden, Layout(major_to_minor=(0, 1)))
    for layer_index in range(section_count):
        params = jax.tree.map(
            lambda mine, theirs: jnp.where(section_index == layer_index, mine, theirs), own, other
        )
        hidden = section_layer(hidden, own_allowed, *params)
    return hidden


def solution(mesh):
    placed = (
        P("dp", None),
        P(),
        P(),
        P("section", "dp"),
        P("section", "dp", "tensor"),
        P("section", "dp", "tensor", None),
        P("section", "tensor", "dp"),
    )
    return jax.shard_map(
        on_device, mesh=mesh, in_specs=placed, out_specs=P("section", "dp"), check_vma=False
    )
```
